256 devices in a mesh: rcv: 16 (over z, core), twin: 16 (over x, y).
Axes of the slice: x: 4, y: 4, z: 8, core: 2. Of those that a mesh axis runs over, the one named last changes fastest.
Arguments:
- record: bfloat16 [4096, 8, 8192], P('rcv', None, 'twin'), may hold values from -6 to 6
- slip_block: int32 [64], P('twin'), may hold values from 16 to 127, as said below
- ghost_lag: int32 [64, 4], P('twin'), may hold values from 1 to 143, as said below
- order_ops: bfloat16 [4, 512, 512], replicated, may hold values from -0.25 to 0.25
Outputs:
- denoised: bfloat16 [4096, 8, 8192], P('rcv', None, 'twin')
The draws below stay inside these ranges and needn't reach their ends.
Inputs may be any that keep to these rules, and one draw needn't show every extreme that they name: `slip_block`: record r begins in a block b with b mod 16 = r // 4 and b // 16 >= 1; the 4 records of one twin index begin in distinct blocks. `ghost_lag`: among the records of one twin index, at most 2 pairs (r, h) with landing >= 0 land on blocks of one twin index; some twin index receives exactly 2 such pairs from every twin index.
All inputs are finite; a program needn't handle non-finite values.
Results may differ from the reference program's by a relative error of at most 0.009.
Values may be sent and summed in bfloat16 or wider, within the bound.
No kernel may reach another device: no remote copies, remote signals or barrier semaphores. Data moves between devices by JAX's collectives and lax.ppermute only.
A program may use at most 128 MiB of HBM per device.

```python
import jax
import jax.numpy as jnp
from jax import lax

PB = 512
NORD = 4
ROUNDS = 8
REC_DEV = 4
CH = 4096
NBLK = 128
NREC = 64
CAP = 2
N_TWIN = 16


def routing_tables(key):
    twin_count = NREC // REC_DEV
    pair_total = REC_DEV * NORD
    base = jax.random.fold_in(key, 811)
    keys = jax.random.split(base, 5)
    hot = jax.random.randint(keys[0], (), 0, twin_count)
    round_scores = jax.random.randint(keys[1], (twin_count, ROUNDS - 1), 0, 1 << 20) * (ROUNDS - 1) + jnp.arange(ROUNDS - 1)
    slip_round = jnp.argsort(round_scores, axis=1)[:, :REC_DEV] + 1
    device = jnp.arange(twin_count)[:, None]
    slip = slip_round * twin_count + device
    pair_scores = jax.random.randint(keys[2], (twin_count, pair_total), 0, 1 << 20) * pair_total + jnp.arange(pair_total)
    rank = jnp.argsort(jnp.argsort(pair_scores, axis=1), axis=1)
    other_scores = jax.random.randint(keys[3], (twin_count, twin_count - 1), 0, 1 << 20) * (twin_count - 1) + jnp.arange(twin_count - 1)
    others = (hot + 1 + jnp.argsort(other_scores, axis=1)) % twin_count
    later = jnp.maximum(rank - CAP, 0) % (twin_count - 1)
    dest_dev = jnp.where(rank < CAP, hot, jnp.take_along_axis(others, later, axis=1))
    pair_round = jnp.repeat(slip_round, NORD, axis=1)
    pair_slip = jnp.repeat(slip, NORD, axis=1)
    lowest = jnp.where(rank < CAP, 0, -1)
    dest_round = jax.random.randint(keys[4], (twin_count, pair_total), lowest, pair_round)
    lag = pair_slip - (dest_round * twin_count + dest_dev)
    forced = (device == twin_count - 1) & (rank == pair_total - 1)
    lag = jnp.where(forced, (ROUNDS + 1) * twin_count - 1, lag)
    return (slip.reshape(NREC).astype(jnp.int32), lag.reshape(NREC, NORD).astype(jnp.int32))


def draw_slip_block(key, part):
    return routing_tables(key)[0]


def draw_ghost_lag(key, part):
    return routing_tables(key)[1]


def level_of(own_key, extent, cuts, smallest, largest):
    def one(axis_at, shards_of):
        steps = jax.random.uniform(jax.random.fold_in(jax.random.fold_in(own_key, 6), axis_at), (shards_of,), jnp.float32, smallest / len(cuts), largest / len(cuts))
        return jnp.repeat(jnp.exp(steps), extent[axis_at] // shards_of).reshape((-1,) + (1,) * (len(extent) - axis_at - 1))

    level = one(*cuts[0])
    for cut in cuts[1:]:
        level = level * one(*cut)
    return level


def normal_values(own_key, dims, deviation, most, cuts=(), held_as=jnp.bfloat16):
    factor_of = level_of(own_key, dims, cuts, -0.22, 0.18) if cuts else 1.0
    drawn = jax.random.normal(own_key, dims, jnp.float32) * deviation * factor_of
    return jnp.minimum(jnp.maximum(drawn, -most), most).astype(held_as)


def setup_inputs(seed: int = 0) -> dict:
    key_list = jax.random.split(jax.random.key(seed), 5)
    return {
        "record": normal_values(key_list[0], (CH, ROUNDS, N_TWIN * PB), 1.0, 6.0, ((0, 16), (2, 16))),
        "slip_block": draw_slip_block(jax.random.fold_in(key_list[4], 71), 0),
        "ghost_lag": draw_ghost_lag(jax.random.fold_in(key_list[4], 71), 0),
        "order_ops": normal_values(key_list[3], (NORD, PB, PB), PB ** -0.5, 0.25),
    }


def reference(record, slip_block, ghost_lag, order_ops):
    channels = record.shape[0]
    blocks = record.reshape(channels, NBLK, PB)
    pair_total = NREC * NORD

    def add_pair(noise, index):
        rec_index = index // NORD
        order_index = index % NORD
        slip = slip_block[rec_index].astype(jnp.int32)
        target = (slip - ghost_lag[rec_index, order_index]).astype(jnp.int32)
        guide = lax.dynamic_slice_in_dim(blocks, slip, 1, 1)[:, 0, :]
        operator = lax.dynamic_index_in_dim(order_ops, order_index, 0, keepdims=False)
        estimate = jnp.dot(guide, operator, preferred_element_type=jnp.float32)
        estimate = lax.optimization_barrier(estimate.astype(jnp.bfloat16)).astype(jnp.float32)
        place = jnp.maximum(target, 0).astype(jnp.int32)
        current = lax.dynamic_slice_in_dim(noise, place, 1, 1)
        update = current + jnp.where(target >= 0, estimate, jnp.zeros_like(estimate))[:, None, :]
        return lax.dynamic_update_slice_in_dim(noise, update, place, 1), None

    start = jnp.zeros((channels, NBLK, PB), jnp.float32)
    noise, _ = lax.scan(add_pair, start, jnp.arange(pair_total, dtype=jnp.int32))
    cleaned = lax.optimization_barrier((blocks.astype(jnp.float32) - noise).astype(jnp.bfloat16)).astype(jnp.float32)
    padded = jnp.pad(cleaned, ((1, 1), (0, 0), (0, 0)))
    smooth = 0.5 * cleaned + 0.25 * (padded[:-2] + padded[2:])
    return smooth.astype(jnp.bfloat16).reshape(channels, ROUNDS, N_TWIN * PB)
```

```python
import jax
import jax.numpy as jnp
from jax import lax
from jax.sharding import PartitionSpec as P


def with_halo(block, sides, width):
    for axis, dim in sides:
        count = lax.axis_size(axis)
        forward = [(i, i + 1) for i in range(count - 1)]
        backward = [(target, source) for source, target in forward]
        low = lax.ppermute(
            lax.slice_in_dim(block, block.shape[dim] - width, None, axis=dim), axis, forward
        )
        high = lax.ppermute(lax.slice_in_dim(block, 0, width, axis=dim), axis, backward)
        block = jnp.concatenate([low, block, high], axis=dim)
    return block


def pair_routes(slip_block, ghost_lag, twin_count):
    rec_count, order_count = ghost_lag.shape
    pair_total = rec_count * order_count
    target = (slip_block[:, None] - ghost_lag).reshape(pair_total)
    valid = target >= 0
    safe = jnp.maximum(target, 0)
    owner = jnp.where(valid, safe % twin_count, -1)
    land_round = safe // twin_count
    position = jnp.arange(pair_total, dtype=jnp.int32)
    earlier = (owner[None, :] == owner[:, None]) & (position[None, :] < position[:, None])
    slot = jnp.sum(earlier.astype(jnp.int32), axis=1)
    return owner, slot, land_round


def local(record, slip_block, ghost_lag, order_ops):
    twin_count = lax.axis_size("twin")
    me = lax.axis_index("twin")
    channels, rounds, samples = record.shape
    rec_count, order_count = ghost_lag.shape
    pair_total = rec_count * order_count
    slot_count = pair_total // twin_count + 1

    table = jnp.concatenate([slip_block, ghost_lag.reshape(pair_total)])
    tables = lax.all_gather(table, "twin")

    guides = jnp.take(record, slip_block // twin_count, axis=1)
    estimates = jnp.einsum(
        "crp,hpq->rhcq", guides, order_ops, preferred_element_type=jnp.float32
    ).astype(jnp.bfloat16)
    estimates = estimates.reshape(pair_total, channels, samples)

    owner, slot, _ = pair_routes(slip_block, ghost_lag, twin_count)
    chosen = (owner[:, None, None] == jnp.arange(twin_count, dtype=jnp.int32)[None, :, None]) & (
        slot[:, None, None] == jnp.arange(slot_count, dtype=jnp.int32)[None, None, :]
    )
    outgoing = jnp.einsum(
        "kns,kcq->nscq", chosen.astype(jnp.bfloat16), estimates, preferred_element_type=jnp.float32
    ).astype(jnp.bfloat16)
    arrived = lax.all_to_all(outgoing, "twin", split_axis=0, concat_axis=0, tiled=True)

    src_slip = tables[:, :rec_count]
    src_lag = tables[:, rec_count:].reshape(twin_count, rec_count, order_count)
    src_owner, src_slot, src_round = jax.vmap(pair_routes, in_axes=(0, 0, None))(
        src_slip, src_lag, twin_count
    )
    mine = src_owner == me
    hit = (
        mine[:, :, None, None]
        & (src_slot[:, :, None, None] == jnp.arange(slot_count, dtype=jnp.int32)[None, None, :, None])
        & (src_round[:, :, None, None] == jnp.arange(rounds, dtype=jnp.int32)[None, None, None, :])
    )
    hit = jnp.sum(hit.astype(jnp.int32), axis=1).astype(jnp.bfloat16)
    noise = jnp.einsum("nsr,nscq->crq", hit, arrived, preferred_element_type=jnp.float32)

    cleaned = (record.astype(jnp.float32) - noise).astype(jnp.bfloat16)
    padded = with_halo(cleaned, (("rcv", 0),), 1)
    widened = padded.astype(jnp.float32)
    smooth = 0.5 * widened[1:-1] + 0.25 * (widened[:-2] + widened[2:])
    return smooth.astype(jnp.bfloat16)


def solution(mesh):
    placed = (P("rcv", None, "twin"), P("twin"), P("twin", None), P())
    return jax.shard_map(
        local, mesh=mesh, in_specs=placed, out_specs=P("rcv", None, "twin"), check_vma=False
    )
```

```python
import jax
import jax.numpy as jnp
from jax import lax
from jax.sharding import PartitionSpec as P


def pair_routes(slip_block, ghost_lag, twin_count):
    rec_count, order_count = ghost_lag.shape
    pair_total = rec_count * order_count
    target = (slip_block[:, None] - ghost_lag).reshape(pair_total)
    valid = target >= 0
    safe = jnp.maximum(target, 0)
    owner = jnp.where(valid, safe % twin_count, -1)
    land_round = safe // twin_count
    position = jnp.arange(pair_total, dtype=jnp.int32)
    earlier = (owner[None, :] == owner[:, None]) & (position[None, :] < position[:, None])
    slot = jnp.sum(earlier.astype(jnp.int32), axis=1)
    return owner, slot, land_round


def local(record, slip_block, ghost_lag, order_ops):
    twin_count = lax.axis_size("twin")
    channels, rounds, samples = record.shape
    rec_count, order_count = ghost_lag.shape
    pair_total = rec_count * order_count
    slot_count = pair_total // twin_count + 1

    guides = jnp.take(record, slip_block // twin_count, axis=1, mode="clip")
    estimates = jnp.einsum(
        "crp,hpq->rhcq", guides, order_ops, preferred_element_type=jnp.float32
    ).astype(jnp.bfloat16)
    estimates = estimates.reshape(pair_total, channels, samples)

    owner, slot, land_round = pair_routes(slip_block, ghost_lag, twin_count)
    meta_rows = 8
    meta = jnp.broadcast_to(land_round.astype(jnp.bfloat16)[:, None, None], (pair_total, meta_rows, samples))
    blank = jnp.zeros((1, channels + meta_rows, samples), jnp.bfloat16)
    tagged = jnp.concatenate([jnp.concatenate([estimates, meta], axis=1), blank], axis=0)
    chosen = (owner[:, None, None] == jnp.arange(twin_count, dtype=jnp.int32)[None, :, None]) & (
        slot[:, None, None] == jnp.arange(slot_count, dtype=jnp.int32)[None, None, :]
    )
    pick = jnp.where(jnp.any(chosen, axis=0), jnp.argmax(chosen, axis=0), pair_total)
    outgoing = jnp.take(tagged, pick.reshape(twin_count * slot_count), axis=0, mode="clip")
    outgoing = outgoing.reshape(twin_count, slot_count * (channels + meta_rows), samples)
    arrived = lax.all_to_all(outgoing, "twin", split_axis=0, concat_axis=0, tiled=True)
    arrived = arrived.reshape(twin_count, slot_count, channels + meta_rows, samples)

    arrived_rounds = arrived[:, :, channels, 0].astype(jnp.int32)
    hit = (arrived_rounds[:, :, None] == jnp.arange(rounds, dtype=jnp.int32)[None, None, :]).astype(jnp.bfloat16)

    def cleaned_rows(lo, hi):
        noise = jnp.einsum(
            "nsr,nscq->crq", hit, arrived[:, :, lo:hi], preferred_element_type=jnp.float32
        )
        return (record[lo:hi].astype(jnp.float32) - noise).astype(jnp.bfloat16)

    count = lax.axis_size("rcv")
    forward = [(i, i + 1) for i in range(count - 1)]
    backward = [(target, source) for source, target in forward]
    low = lax.ppermute(cleaned_rows(channels - 1, channels), "rcv", forward)
    high = lax.ppermute(cleaned_rows(0, 1), "rcv", backward)
    cleaned = cleaned_rows(0, channels)
    widened = jnp.concatenate([low, cleaned, high], axis=0).astype(jnp.float32)
    smooth = 0.5 * widened[1:-1] + 0.25 * (widened[:-2] + widened[2:])
    return smooth.astype(jnp.bfloat16)


def solution(mesh):
    placed = (P("rcv", None, "twin"), P("twin"), P("twin", None), P())
    return jax.shard_map(
        local, mesh=mesh, in_specs=placed, out_specs=P("rcv", None, "twin"), check_vma=False
    )
```

```python
import jax
import jax.numpy as jnp
from jax import lax
from jax.sharding import PartitionSpec as P


def pair_routes(slip_block, ghost_lag, twin_count):
    rec_count, order_count = ghost_lag.shape
    pair_total = rec_count * order_count
    target = (slip_block[:, None] - ghost_lag).reshape(pair_total)
    valid = target >= 0
    safe = jnp.maximum(target, 0)
    owner = jnp.where(valid, safe % twin_count, -1)
    land_round = safe // twin_count
    position = jnp.arange(pair_total, dtype=jnp.int32)
    earlier = (owner[None, :] == owner[:, None]) & (position[None, :] < position[:, None])
    slot = jnp.sum(earlier.astype(jnp.int32), axis=1)
    return owner, slot, land_round


def local(record, slip_block, ghost_lag, order_ops):
    twin_count = lax.axis_size("twin")
    channels, rounds, samples = record.shape
    rec_count, order_count = ghost_lag.shape
    pair_total = rec_count * order_count
    slot_count = pair_total // twin_count + 1

    guides = jnp.take(record, slip_block // twin_count, axis=1, mode="clip")
    estimates = jnp.einsum(
        "crp,hpq->rhcq", guides, order_ops, preferred_element_type=jnp.float32
    ).astype(jnp.bfloat16)
    estimates = estimates.reshape(pair_total, channels, samples)

    owner, slot, land_round = pair_routes(slip_block, ghost_lag, twin_count)
    meta_rows = 8
    meta = jnp.broadcast_to(land_round.astype(jnp.bfloat16)[:, None, None], (pair_total, meta_rows, samples))
    blank = jnp.zeros((1, channels + meta_rows, samples), jnp.bfloat16)
    tagged = jnp.concatenate([jnp.concatenate([estimates, meta], axis=1), blank], axis=0)
    chosen = (owner[:, None, None] == jnp.arange(twin_count, dtype=jnp.int32)[None, :, None]) & (
        slot[:, None, None] == jnp.arange(slot_count, dtype=jnp.int32)[None, None, :]
    )
    pick = jnp.where(jnp.any(chosen, axis=0), jnp.argmax(chosen, axis=0), pair_total)
    outgoing = jnp.take(tagged, pick.reshape(twin_count * slot_count), axis=0, mode="clip")
    outgoing = outgoing.reshape(twin_count, slot_count * (channels + meta_rows), samples)
    arrived = lax.all_to_all(outgoing, "twin", split_axis=0, concat_axis=0, tiled=True)
    arrived = arrived.reshape(twin_count, slot_count, channels + meta_rows, samples)

    arrived_rounds = arrived[:, :, channels, 0].astype(jnp.int32)
    hit = (arrived_rounds[:, :, None] == jnp.arange(rounds, dtype=jnp.int32)[None, None, :]).astype(jnp.bfloat16)

    noise = jnp.einsum("nsr,nscq->crq", hit, arrived, preferred_element_type=jnp.float32)

    def cleaned_rows(lo, hi):
        return (record[lo:hi].astype(jnp.float32) - noise[lo:hi]).astype(jnp.bfloat16)

    count = lax.axis_size("rcv")
    forward = [(i, i + 1) for i in range(count - 1)]
    backward = [(target, source) for source, target in forward]
    low = lax.ppermute(cleaned_rows(channels - 1, channels), "rcv", forward)
    high = lax.ppermute(cleaned_rows(0, 1), "rcv", backward)
    cleaned = cleaned_rows(0, channels)
    widened = jnp.concatenate([low, cleaned, high], axis=0).astype(jnp.float32)
    smooth = 0.5 * widened[1:-1] + 0.25 * (widened[:-2] + widened[2:])
    return smooth.astype(jnp.bfloat16)


def solution(mesh):
    placed = (P("rcv", None, "twin"), P("twin"), P("twin", None), P())
    return jax.shard_map(
        local, mesh=mesh, in_specs=placed, out_specs=P("rcv", None, "twin"), check_vma=False
    )
```

```python
import jax
import jax.numpy as jnp
from jax import lax
from jax.sharding import PartitionSpec as P


def pair_routes(slip_block, ghost_lag, twin_count):
    rec_count, order_count = ghost_lag.shape
    pair_total = rec_count * order_count
    target = (slip_block[:, None] - ghost_lag).reshape(pair_total)
    valid = target >= 0
    safe = jnp.maximum(target, 0)
    owner = jnp.where(valid, safe % twin_count, -1)
    land_round = safe // twin_count
    position = jnp.arange(pair_total, dtype=jnp.int32)
    earlier = (owner[None, :] == owner[:, None]) & (position[None, :] < position[:, None])
    slot = jnp.sum(earlier.astype(jnp.int32), axis=1)
    return owner, slot, land_round


def local(record, slip_block, ghost_lag, order_ops):
    twin_count = lax.axis_size("twin")
    channels, rounds, samples = record.shape
    rec_count, order_count = ghost_lag.shape
    pair_total = rec_count * order_count
    slot_count = pair_total // twin_count + 1

    planes = jnp.transpose(record, (1, 0, 2))

    guides = jnp.take(planes, slip_block // twin_count, axis=0, mode="clip")
    estimates = jnp.einsum(
        "rcp,hpq->rhcq", guides, order_ops, preferred_element_type=jnp.float32
    ).astype(jnp.bfloat16)
    estimates = estimates.reshape(pair_total, channels, samples)

    owner, slot, land_round = pair_routes(slip_block, ghost_lag, twin_count)
    meta_rows = 8
    meta = jnp.broadcast_to(land_round.astype(jnp.bfloat16)[:, None, None], (pair_total, meta_rows, samples))
    blank = jnp.zeros((1, channels + meta_rows, samples), jnp.bfloat16)
    tagged = jnp.concatenate([jnp.concatenate([estimates, meta], axis=1), blank], axis=0)
    chosen = (owner[:, None, None] == jnp.arange(twin_count, dtype=jnp.int32)[None, :, None]) & (
        slot[:, None, None] == jnp.arange(slot_count, dtype=jnp.int32)[None, None, :]
    )
    pick = jnp.where(jnp.any(chosen, axis=0), jnp.argmax(chosen, axis=0), pair_total)
    outgoing = jnp.take(tagged, pick.reshape(twin_count * slot_count), axis=0, mode="clip")
    outgoing = outgoing.reshape(twin_count, slot_count * (channels + meta_rows), samples)
    arrived = lax.all_to_all(outgoing, "twin", split_axis=0, concat_axis=0, tiled=True)
    arrived = arrived.reshape(twin_count, slot_count, channels + meta_rows, samples)

    arrived_rounds = arrived[:, :, channels, 0].astype(jnp.int32)
    hit = (arrived_rounds[:, :, None] == jnp.arange(rounds, dtype=jnp.int32)[None, None, :]).astype(jnp.bfloat16)
    noise = jnp.einsum("nsr,nscq->rcq", hit, arrived, preferred_element_type=jnp.float32)

    def cleaned_rows(lo, hi):
        return (planes[:, lo:hi].astype(jnp.float32) - noise[:, lo:hi]).astype(jnp.bfloat16)

    count = lax.axis_size("rcv")
    forward = [(i, i + 1) for i in range(count - 1)]
    backward = [(target, source) for source, target in forward]
    low = lax.ppermute(cleaned_rows(channels - 1, channels), "rcv", forward)
    high = lax.ppermute(cleaned_rows(0, 1), "rcv", backward)
    cleaned = cleaned_rows(0, channels)
    widened = jnp.concatenate([low, cleaned, high], axis=1).astype(jnp.float32)
    smooth = 0.5 * widened[:, 1:-1] + 0.25 * (widened[:, :-2] + widened[:, 2:])
    return jnp.transpose(smooth.astype(jnp.bfloat16), (1, 0, 2))


def solution(mesh):
    placed = (P("rcv", None, "twin"), P("twin"), P("twin", None), P())
    return jax.shard_map(
        local, mesh=mesh, in_specs=placed, out_specs=P("rcv", None, "twin"), check_vma=False
    )
```

```python
import jax
import jax.numpy as jnp
from jax import lax
from jax.sharding import PartitionSpec as P


def pair_routes(slip_block, ghost_lag, twin_count):
    rec_count, order_count = ghost_lag.shape
    pair_total = rec_count * order_count
    target = (slip_block[:, None] - ghost_lag).reshape(pair_total)
    valid = target >= 0
    safe = jnp.maximum(target, 0)
    owner = jnp.where(valid, safe % twin_count, -1)
    land_round = safe // twin_count
    position = jnp.arange(pair_total, dtype=jnp.int32)
    earlier = (owner[None, :] == owner[:, None]) & (position[None, :] < position[:, None])
    slot = jnp.sum(earlier.astype(jnp.int32), axis=1)
    return owner, slot, land_round


def local(record, slip_block, ghost_lag, order_ops):
    twin_count = lax.axis_size("twin")
    channels, rounds, samples = record.shape
    rec_count, order_count = ghost_lag.shape
    pair_total = rec_count * order_count
    slot_count = pair_total // twin_count + 1

    guides = jnp.take(record, slip_block // twin_count, axis=1, mode="clip")
    estimates = jnp.einsum(
        "crp,hpq->rhcq", guides, order_ops, preferred_element_type=jnp.float32
    ).astype(jnp.bfloat16)
    estimates = estimates.reshape(pair_total, channels, samples)

    owner, slot, land_round = pair_routes(slip_block, ghost_lag, twin_count)
    meta_rows = 8
    meta = jnp.broadcast_to(land_round.astype(jnp.bfloat16)[:, None, None], (pair_total, meta_rows, samples))
    blank = jnp.zeros((1, channels + meta_rows, samples), jnp.bfloat16)
    tagged = jnp.concatenate([jnp.concatenate([estimates, meta], axis=1), blank], axis=0)
    chosen = (owner[:, None, None] == jnp.arange(twin_count, dtype=jnp.int32)[None, :, None]) & (
        slot[:, None, None] == jnp.arange(slot_count, dtype=jnp.int32)[None, None, :]
    )
    pick = jnp.where(jnp.any(chosen, axis=0), jnp.argmax(chosen, axis=0), pair_total)
    outgoing = jnp.take(tagged, pick.reshape(twin_count * slot_count), axis=0, mode="clip")
    outgoing = outgoing.reshape(twin_count, slot_count * (channels + meta_rows), samples)
    arrived = lax.all_to_all(outgoing, "twin", split_axis=0, concat_axis=0, tiled=True)
    arrived = arrived.reshape(twin_count, slot_count, channels + meta_rows, samples)

    arrived_rounds = arrived[:, :, channels, 0].astype(jnp.int32)
    hit = (arrived_rounds[:, :, None] == jnp.arange(rounds, dtype=jnp.int32)[None, None, :]).astype(jnp.bfloat16)

    sub = 8
    blocks = (channels + meta_rows) // sub
    spread = jnp.einsum(
        "jr,ik->irjk", hit.reshape(twin_count * slot_count, rounds), jnp.eye(sub, dtype=jnp.bfloat16)
    )
    stacked = arrived.reshape(twin_count * slot_count, blocks, sub, samples)
    noise = jnp.einsum("irjk,jbkq->birq", spread, stacked, preferred_element_type=jnp.float32)
    noise = noise.reshape(blocks * sub, rounds, samples)

    def cleaned_rows(lo, hi):
        return (record[lo:hi].astype(jnp.float32) - noise[lo:hi]).astype(jnp.bfloat16)

    count = lax.axis_size("rcv")
    forward = [(i, i + 1) for i in range(count - 1)]
    backward = [(target, source) for source, target in forward]
    low = lax.ppermute(cleaned_rows(channels - 1, channels), "rcv", forward)
    high = lax.ppermute(cleaned_rows(0, 1), "rcv", backward)
    cleaned = cleaned_rows(0, channels)
    widened = jnp.concatenate([low, cleaned, high], axis=0).astype(jnp.float32)
    smooth = 0.5 * widened[1:-1] + 0.25 * (widened[:-2] + widened[2:])
    return smooth.astype(jnp.bfloat16)


def solution(mesh):
    placed = (P("rcv", None, "twin"), P("twin"), P("twin", None), P())
    return jax.shard_map(
        local, mesh=mesh, in_specs=placed, out_specs=P("rcv", None, "twin"), check_vma=False
    )
```

```python
import jax
import jax.numpy as jnp
from jax import lax
from jax.sharding import PartitionSpec as P


def pair_routes(slip_block, ghost_lag, twin_count):
    rec_count, order_count = ghost_lag.shape
    pair_total = rec_count * order_count
    target = (slip_block[:, None] - ghost_lag).reshape(pair_total)
    valid = target >= 0
    safe = jnp.maximum(target, 0)
    owner = jnp.where(valid, safe % twin_count, -1)
    land_round = safe // twin_count
    position = jnp.arange(pair_total, dtype=jnp.int32)
    earlier = (owner[None, :] == owner[:, None]) & (position[None, :] < position[:, None])
    slot = jnp.sum(earlier.astype(jnp.int32), axis=1)
    return owner, slot, land_round


def local(record, slip_block, ghost_lag, order_ops):
    twin_count = lax.axis_size("twin")
    channels, rounds, samples = record.shape
    rec_count, order_count = ghost_lag.shape
    pair_total = rec_count * order_count
    slot_count = pair_total // twin_count + 1

    guides = jnp.take(record, slip_block // twin_count, axis=1, mode="clip")
    estimates = jnp.einsum(
        "crp,hpq->rhcq", guides, order_ops, preferred_element_type=jnp.float32
    ).astype(jnp.bfloat16)
    estimates = estimates.reshape(pair_total, channels, samples)

    owner, slot, land_round = pair_routes(slip_block, ghost_lag, twin_count)
    meta_rows = 8
    meta = jnp.broadcast_to(land_round.astype(jnp.bfloat16)[:, None, None], (pair_total, meta_rows, samples))
    blank = jnp.zeros((1, channels + meta_rows, samples), jnp.bfloat16)
    tagged = jnp.concatenate([jnp.concatenate([estimates, meta], axis=1), blank], axis=0)
    chosen = (owner[:, None, None] == jnp.arange(twin_count, dtype=jnp.int32)[None, :, None]) & (
        slot[:, None, None] == jnp.arange(slot_count, dtype=jnp.int32)[None, None, :]
    )
    pick = jnp.where(jnp.any(chosen, axis=0), jnp.argmax(chosen, axis=0), pair_total)
    outgoing = jnp.take(tagged, pick.reshape(twin_count * slot_count), axis=0, mode="clip")
    outgoing = outgoing.reshape(twin_count, slot_count * (channels + meta_rows), samples)
    sub = 8
    same = lax.broadcasted_iota(jnp.int32, (sub, 1, 1, sub), 0) == lax.broadcasted_iota(jnp.int32, (sub, 1, 1, sub), 3)
    outgoing, same = lax.optimization_barrier((outgoing, same))
    arrived = lax.all_to_all(outgoing, "twin", split_axis=0, concat_axis=0, tiled=True)
    arrived = arrived.reshape(twin_count, slot_count, channels + meta_rows, samples)

    arrived_rounds = arrived[:, :, channels, 0].astype(jnp.int32)
    hit = (arrived_rounds[:, :, None] == jnp.arange(rounds, dtype=jnp.int32)[None, None, :]).astype(jnp.bfloat16)

    sub = 8
    blocks = (channels + meta_rows) // sub
    spread = jnp.where(same, hit.reshape(twin_count * slot_count, rounds).T[None, :, :, None], jnp.zeros((), jnp.bfloat16))
    stacked = arrived.reshape(twin_count * slot_count, blocks, sub, samples)
    noise = jnp.einsum("irjk,jbkq->birq", spread, stacked, preferred_element_type=jnp.float32)
    noise = noise.reshape(blocks * sub, rounds, samples)

    def cleaned_rows(lo, hi):
        return (record[lo:hi].astype(jnp.float32) - noise[lo:hi]).astype(jnp.bfloat16)

    count = lax.axis_size("rcv")
    forward = [(i, i + 1) for i in range(count - 1)]
    backward = [(target, source) for source, target in forward]
    low = lax.ppermute(cleaned_rows(channels - 1, channels), "rcv", forward)
    high = lax.ppermute(cleaned_rows(0, 1), "rcv", backward)
    cleaned = cleaned_rows(0, channels)
    widened = jnp.concatenate([low, cleaned, high], axis=0).astype(jnp.float32)
    smooth = 0.5 * widened[1:-1] + 0.25 * (widened[:-2] + widened[2:])
    return smooth.astype(jnp.bfloat16)


def solution(mesh):
    placed = (P("rcv", None, "twin"), P("twin"), P("twin", None), P())
    return jax.shard_map(
        local, mesh=mesh, in_specs=placed, out_specs=P("rcv", None, "twin"), check_vma=False
    )
```

```python
import jax
import jax.numpy as jnp
from jax import lax
from jax.sharding import PartitionSpec as P


def pair_routes(slip_block, ghost_lag, twin_count):
    rec_count, order_count = ghost_lag.shape
    pair_total = rec_count * order_count
    target = (slip_block[:, None] - ghost_lag).reshape(pair_total)
    valid = target >= 0
    safe = jnp.maximum(target, 0)
    owner = jnp.where(valid, safe % twin_count, -1)
    land_round = safe // twin_count
    position = jnp.arange(pair_total, dtype=jnp.int32)
    earlier = (owner[None, :] == owner[:, None]) & (position[None, :] < position[:, None])
    slot = jnp.sum(earlier.astype(jnp.int32), axis=1)
    return owner, slot, land_round


def local(record, slip_block, ghost_lag, order_ops):
    twin_count = lax.axis_size("twin")
    channels, rounds, samples = record.shape
    rec_count, order_count = ghost_lag.shape
    pair_total = rec_count * order_count
    slot_count = pair_total // twin_count + 1

    guides = jnp.take(record, slip_block // twin_count, axis=1, mode="clip")
    estimates = jnp.einsum(
        "crp,hpq->rhcq", guides, order_ops, preferred_element_type=jnp.float32
    ).astype(jnp.bfloat16)
    estimates = estimates.reshape(pair_total, channels, samples)

    owner, slot, land_round = pair_routes(slip_block, ghost_lag, twin_count)
    meta_rows = 8
    meta = jnp.broadcast_to(land_round.astype(jnp.bfloat16)[:, None, None], (pair_total, meta_rows, samples))
    blank = jnp.zeros((1, channels + meta_rows, samples), jnp.bfloat16)
    tagged = jnp.concatenate([jnp.concatenate([estimates, meta], axis=1), blank], axis=0)
    chosen = (owner[:, None, None] == jnp.arange(twin_count, dtype=jnp.int32)[None, :, None]) & (
        slot[:, None, None] == jnp.arange(slot_count, dtype=jnp.int32)[None, None, :]
    )
    pick = jnp.where(jnp.any(chosen, axis=0), jnp.argmax(chosen, axis=0), pair_total)
    outgoing = jnp.take(tagged, pick.reshape(twin_count * slot_count), axis=0, mode="clip")
    outgoing = outgoing.reshape(twin_count, slot_count * (channels + meta_rows), samples)
    sub = 8
    same = lax.broadcasted_iota(jnp.int32, (sub, 1, 1, sub), 0) == lax.broadcasted_iota(jnp.int32, (sub, 1, 1, sub), 3)
    outgoing, same = lax.optimization_barrier((outgoing, same))
    arrived = lax.all_to_all(outgoing, "twin", split_axis=0, concat_axis=0, tiled=True)
    arrived = arrived.reshape(twin_count, slot_count, channels + meta_rows, samples)

    arrived_rounds = arrived[:, :, channels, 0].astype(jnp.int32)
    hit = (arrived_rounds[:, :, None] == jnp.arange(rounds, dtype=jnp.int32)[None, None, :]).astype(jnp.bfloat16)

    sub = 8
    blocks = (channels + meta_rows) // sub
    spread = jnp.where(same, hit.reshape(twin_count * slot_count, rounds).T[None, :, :, None], jnp.zeros((), jnp.bfloat16))
    stacked = arrived.reshape(twin_count * slot_count, blocks, sub, samples)
    noise = jnp.einsum("irjk,jbkq->birq", spread, stacked, preferred_element_type=jnp.float32)
    noise = noise.reshape(blocks * sub, rounds, samples)

    def cleaned_rows(lo, hi):
        return (record[lo:hi].astype(jnp.float32) - noise[lo:hi]).astype(jnp.bfloat16)

    def edge_row(c):
        edge_noise = jnp.einsum(
            "nsr,nsq->rq", hit, arrived[:, :, c], preferred_element_type=jnp.float32
        )
        return (record[c].astype(jnp.float32) - edge_noise).astype(jnp.bfloat16)[None]

    count = lax.axis_size("rcv")
    forward = [(i, i + 1) for i in range(count - 1)]
    backward = [(target, source) for source, target in forward]
    low = lax.ppermute(edge_row(channels - 1), "rcv", forward)
    high = lax.ppermute(edge_row(0), "rcv", backward)
    cleaned = cleaned_rows(0, channels)
    widened = jnp.concatenate([low, cleaned, high], axis=0).astype(jnp.float32)
    smooth = 0.5 * widened[1:-1] + 0.25 * (widened[:-2] + widened[2:])
    return smooth.astype(jnp.bfloat16)


def solution(mesh):
    placed = (P("rcv", None, "twin"), P("twin"), P("twin", None), P())
    return jax.shard_map(
        local, mesh=mesh, in_specs=placed, out_specs=P("rcv", None, "twin"), check_vma=False
    )
```

```python
import jax
import jax.numpy as jnp
from jax import lax
from jax.sharding import PartitionSpec as P


def pair_routes(slip_block, ghost_lag, twin_count):
    rec_count, order_count = ghost_lag.shape
    pair_total = rec_count * order_count
    target = (slip_block[:, None] - ghost_lag).reshape(pair_total)
    valid = target >= 0
    safe = jnp.maximum(target, 0)
    owner = jnp.where(valid, safe % twin_count, -1)
    land_round = safe // twin_count
    position = jnp.arange(pair_total, dtype=jnp.int32)
    earlier = (owner[None, :] == owner[:, None]) & (position[None, :] < position[:, None])
    slot = jnp.sum(earlier.astype(jnp.int32), axis=1)
    return owner, slot, land_round


def local(record, slip_block, ghost_lag, order_ops):
    twin_count = lax.axis_size("twin")
    channels, rounds, samples = record.shape
    rec_count, order_count = ghost_lag.shape
    pair_total = rec_count * order_count
    slot_count = pair_total // twin_count + 1

    slip_round = slip_block // twin_count
    on_round = slip_round[:, None] == jnp.arange(rounds, dtype=jnp.int32)[None, :]
    guides = jnp.sum(
        jnp.where(on_round[None, :, :, None], record[:, None, :, :], jnp.zeros((), record.dtype)), axis=2
    )
    estimates = jnp.einsum(
        "crp,hpq->rhcq", guides, order_ops, preferred_element_type=jnp.float32
    ).astype(jnp.bfloat16)
    estimates = estimates.reshape(pair_total, channels, samples)

    owner, slot, land_round = pair_routes(slip_block, ghost_lag, twin_count)
    meta_rows = 8
    meta = jnp.broadcast_to(land_round.astype(jnp.bfloat16)[:, None, None], (pair_total, meta_rows, samples))
    blank = jnp.zeros((1, channels + meta_rows, samples), jnp.bfloat16)
    tagged = jnp.concatenate([jnp.concatenate([estimates, meta], axis=1), blank], axis=0)
    chosen = (owner[:, None, None] == jnp.arange(twin_count, dtype=jnp.int32)[None, :, None]) & (
        slot[:, None, None] == jnp.arange(slot_count, dtype=jnp.int32)[None, None, :]
    )
    pick = jnp.where(jnp.any(chosen, axis=0), jnp.argmax(chosen, axis=0), pair_total)
    outgoing = jnp.take(tagged, pick.reshape(twin_count * slot_count), axis=0, mode="clip")
    outgoing = outgoing.reshape(twin_count, slot_count * (channels + meta_rows), samples)
    sub = 8
    same = lax.broadcasted_iota(jnp.int32, (sub, 1, 1, sub), 0) == lax.broadcasted_iota(jnp.int32, (sub, 1, 1, sub), 3)
    outgoing, same = lax.optimization_barrier((outgoing, same))
    arrived = lax.all_to_all(outgoing, "twin", split_axis=0, concat_axis=0, tiled=True)
    arrived = arrived.reshape(twin_count, slot_count, channels + meta_rows, samples)

    arrived_rounds = arrived[:, :, channels, 0].astype(jnp.int32)
    hit = (arrived_rounds[:, :, None] == jnp.arange(rounds, dtype=jnp.int32)[None, None, :]).astype(jnp.bfloat16)

    sub = 8
    blocks = (channels + meta_rows) // sub
    spread = jnp.where(same, hit.reshape(twin_count * slot_count, rounds).T[None, :, :, None], jnp.zeros((), jnp.bfloat16))
    stacked = arrived.reshape(twin_count * slot_count, blocks, sub, samples)
    noise = jnp.einsum("irjk,jbkq->birq", spread, stacked, preferred_element_type=jnp.float32)
    noise = noise.reshape(blocks * sub, rounds, samples)

    def cleaned_rows(lo, hi):
        return (record[lo:hi].astype(jnp.float32) - noise[lo:hi]).astype(jnp.bfloat16)

    def edge_row(c):
        edge_noise = jnp.einsum(
            "nsr,nsq->rq", hit, arrived[:, :, c], preferred_element_type=jnp.float32
        )
        return (record[c].astype(jnp.float32) - edge_noise).astype(jnp.bfloat16)[None]

    count = lax.axis_size("rcv")
    forward = [(i, i + 1) for i in range(count - 1)]
    backward = [(target, source) for source, target in forward]
    low = lax.ppermute(edge_row(channels - 1), "rcv", forward)
    high = lax.ppermute(edge_row(0), "rcv", backward)
    cleaned = cleaned_rows(0, channels)
    widened = jnp.concatenate([low, cleaned, high], axis=0).astype(jnp.float32)
    smooth = 0.5 * widened[1:-1] + 0.25 * (widened[:-2] + widened[2:])
    return smooth.astype(jnp.bfloat16)


def solution(mesh):
    placed = (P("rcv", None, "twin"), P("twin"), P("twin", None), P())
    return jax.shard_map(
        local, mesh=mesh, in_specs=placed, out_specs=P("rcv", None, "twin"), check_vma=False
    )
```

```python
import jax
import jax.numpy as jnp
from jax import lax
from jax.experimental import pallas as pl
from jax.experimental.pallas import tpu as pltpu
from jax.sharding import PartitionSpec as P


def pair_routes(slip_block, ghost_lag, twin_count):
    rec_count, order_count = ghost_lag.shape
    pair_total = rec_count * order_count
    target = (slip_block[:, None] - ghost_lag).reshape(pair_total)
    valid = target >= 0
    safe = jnp.maximum(target, 0)
    owner = jnp.where(valid, safe % twin_count, -1)
    land_round = safe // twin_count
    position = jnp.arange(pair_total, dtype=jnp.int32)
    earlier = (owner[None, :] == owner[:, None]) & (position[None, :] < position[:, None])
    slot = jnp.sum(earlier.astype(jnp.int32), axis=1)
    return owner, slot, land_round


def place_clean_smooth(spread, arrived, record, channel_block, sub):
    slots, _, samples = arrived.shape
    channels, rounds, _ = record.shape
    steps = channels // channel_block

    def kernel(spread_ref, arrived_ref, record_ref, out_ref, edge_ref, scratch_ref):
        t = pl.program_id(0)
        for g in range(channel_block // sub):
            panel_rows = arrived_ref[:, g * sub : (g + 1) * sub, :].reshape(slots * sub, samples)
            noise = jnp.dot(spread_ref[...], panel_rows, preferred_element_type=jnp.float32)
            noise = noise.reshape(sub, rounds, samples)
            rec = record_ref[g * sub : (g + 1) * sub].astype(jnp.float32)
            cleaned = (rec - noise).astype(jnp.bfloat16).astype(jnp.float32)
            scratch_ref[pl.ds(1 + t * channel_block + g * sub, sub)] = cleaned

        @pl.when(t == steps - 1)
        def _():
            scratch_ref[0] = jnp.zeros((rounds, samples), jnp.float32)
            scratch_ref[channels + 1] = jnp.zeros((rounds, samples), jnp.float32)

            def body(i, carry):
                lo = i * sub
                mid = scratch_ref[pl.ds(lo + 1, sub)]
                up = scratch_ref[pl.ds(lo, sub)]
                down = scratch_ref[pl.ds(lo + 2, sub)]
                out_ref[pl.ds(lo, sub)] = (0.5 * mid + 0.25 * (up + down)).astype(out_ref.dtype)
                return carry

            lax.fori_loop(0, channels // sub, body, 0)
            edge_ref[0:2] = scratch_ref[1:3]
            edge_ref[2:4] = scratch_ref[channels - 1 : channels + 1]

    return pl.pallas_call(
        kernel,
        grid=(steps,),
        in_specs=[
            pl.BlockSpec(spread.shape, lambda t: (0, 0)),
            pl.BlockSpec((slots, channel_block, samples), lambda t: (0, t, 0)),
            pl.BlockSpec((channel_block, rounds, samples), lambda t: (t, 0, 0)),
        ],
        out_specs=[
            pl.BlockSpec((channels, rounds, samples), lambda t: (0, 0, 0)),
            pl.BlockSpec((4, rounds, samples), lambda t: (0, 0, 0)),
        ],
        out_shape=[
            jax.ShapeDtypeStruct((channels, rounds, samples), jnp.bfloat16),
            jax.ShapeDtypeStruct((4, rounds, samples), jnp.float32),
        ],
        scratch_shapes=[pltpu.VMEM((channels + 2, rounds, samples), jnp.float32)],
        compiler_params=pltpu.CompilerParams(dimension_semantics=("arbitrary",)),
    )(spread, arrived, record)


def local(record, slip_block, ghost_lag, order_ops):
    twin_count = lax.axis_size("twin")
    channels, rounds, samples = record.shape
    rec_count, order_count = ghost_lag.shape
    pair_total = rec_count * order_count
    slot_count = pair_total // twin_count + 1

    guides = jnp.take(record, slip_block // twin_count, axis=1, mode="clip")
    estimates = jnp.einsum(
        "crp,hpq->rhcq", guides, order_ops, preferred_element_type=jnp.float32
    ).astype(jnp.bfloat16)
    estimates = estimates.reshape(pair_total, channels, samples)

    owner, slot, land_round = pair_routes(slip_block, ghost_lag, twin_count)
    meta_rows = 8
    meta = jnp.broadcast_to(land_round.astype(jnp.bfloat16)[:, None, None], (pair_total, meta_rows, samples))
    blank = jnp.zeros((1, channels + meta_rows, samples), jnp.bfloat16)
    tagged = jnp.concatenate([jnp.concatenate([estimates, meta], axis=1), blank], axis=0)
    chosen = (owner[:, None, None] == jnp.arange(twin_count, dtype=jnp.int32)[None, :, None]) & (
        slot[:, None, None] == jnp.arange(slot_count, dtype=jnp.int32)[None, None, :]
    )
    pick = jnp.where(jnp.any(chosen, axis=0), jnp.argmax(chosen, axis=0), pair_total)
    outgoing = jnp.take(tagged, pick.reshape(twin_count * slot_count), axis=0, mode="clip")
    outgoing = outgoing.reshape(twin_count, slot_count * (channels + meta_rows), samples)
    sub = 16
    same = lax.broadcasted_iota(jnp.int32, (sub, 1, 1, sub), 0) == lax.broadcasted_iota(jnp.int32, (sub, 1, 1, sub), 3)
    outgoing, same = lax.optimization_barrier((outgoing, same))
    arrived = lax.all_to_all(outgoing, "twin", split_axis=0, concat_axis=0, tiled=True)
    arrived = arrived.reshape(twin_count, slot_count, channels + meta_rows, samples)

    arrived_rounds = arrived[:, :, channels, 0].astype(jnp.int32)
    hit = (arrived_rounds[:, :, None] == jnp.arange(rounds, dtype=jnp.int32)[None, None, :]).astype(jnp.bfloat16)

    spread = jnp.where(same, hit.reshape(twin_count * slot_count, rounds).T[None, :, :, None], jnp.zeros((), jnp.bfloat16))
    spread = spread.reshape(sub * rounds, twin_count * slot_count * sub)

    def edge_row(c):
        edge_noise = jnp.einsum(
            "nsr,nsq->rq", hit, arrived[:, :, c], preferred_element_type=jnp.float32
        )
        return (record[c].astype(jnp.float32) - edge_noise).astype(jnp.bfloat16)[None]

    count = lax.axis_size("rcv")
    forward = [(i, i + 1) for i in range(count - 1)]
    backward = [(target, source) for source, target in forward]
    low = lax.ppermute(edge_row(channels - 1), "rcv", forward)
    high = lax.ppermute(edge_row(0), "rcv", backward)
    slots_view = arrived.reshape(twin_count * slot_count, channels + meta_rows, samples)
    smooth, edges = place_clean_smooth(spread, slots_view, record, 32, sub)
    first = 0.5 * edges[0] + 0.25 * (low[0].astype(jnp.float32) + edges[1])
    last = 0.5 * edges[3] + 0.25 * (edges[2] + high[0].astype(jnp.float32))
    smooth = smooth.at[0].set(first.astype(jnp.bfloat16)).at[channels - 1].set(last.astype(jnp.bfloat16))
    return smooth


def solution(mesh):
    placed = (P("rcv", None, "twin"), P("twin"), P("twin", None), P())
    return jax.shard_map(
        local, mesh=mesh, in_specs=placed, out_specs=P("rcv", None, "twin"), check_vma=False
    )
```

```python
import jax
import jax.numpy as jnp
from jax import lax
from jax.sharding import PartitionSpec as P


def pair_routes(slip_block, ghost_lag, twin_count):
    rec_count, order_count = ghost_lag.shape
    pair_total = rec_count * order_count
    target = (slip_block[:, None] - ghost_lag).reshape(pair_total)
    valid = target >= 0
    safe = jnp.maximum(target, 0)
    owner = jnp.where(valid, safe % twin_count, -1)
    land_round = safe // twin_count
    position = jnp.arange(pair_total, dtype=jnp.int32)
    earlier = (owner[None, :] == owner[:, None]) & (position[None, :] < position[:, None])
    slot = jnp.sum(earlier.astype(jnp.int32), axis=1)
    return owner, slot, land_round


def local(record, slip_block, ghost_lag, order_ops):
    twin_count = lax.axis_size("twin")
    channels, rounds, samples = record.shape
    rec_count, order_count = ghost_lag.shape
    pair_total = rec_count * order_count
    slot_count = pair_total // twin_count + 1

    owner, slot, land_round = pair_routes(slip_block, ghost_lag, twin_count)
    meta_rows = 8
    guides = jnp.take(record, slip_block // twin_count, axis=1, mode="clip")
    guides = jnp.pad(guides, ((0, meta_rows), (0, 0), (0, 0)))
    tags = jnp.stack([land_round, owner, slot], axis=1).astype(jnp.float32)
    tags = jnp.pad(tags, ((0, 0), (channels, meta_rows - tags.shape[1])))
    tags = tags.reshape(rec_count, order_count, channels + meta_rows)[:, :, :, None]
    estimates = (
        jnp.einsum("crp,hpq->rhcq", guides, order_ops, preferred_element_type=jnp.float32) + tags
    ).astype(jnp.bfloat16)
    tagged = estimates.reshape(pair_total, channels + meta_rows, samples)
    chosen = (owner[:, None, None] == jnp.arange(twin_count, dtype=jnp.int32)[None, :, None]) & (
        slot[:, None, None] == jnp.arange(slot_count, dtype=jnp.int32)[None, None, :]
    )
    pick = jnp.argmax(chosen, axis=0)
    outgoing = jnp.take(tagged, pick.reshape(twin_count * slot_count), axis=0, mode="clip")
    outgoing = outgoing.reshape(twin_count, slot_count * (channels + meta_rows), samples)
    sub = 8
    same = lax.broadcasted_iota(jnp.int32, (sub, 1, 1, sub), 0) == lax.broadcasted_iota(jnp.int32, (sub, 1, 1, sub), 3)
    me = lax.axis_index("twin")
    outgoing, same, me = lax.optimization_barrier((outgoing, same, me))
    arrived = lax.all_to_all(outgoing, "twin", split_axis=0, concat_axis=0, tiled=True)
    arrived = arrived.reshape(twin_count, slot_count, channels + meta_rows, samples)

    arrived_tags = arrived[:, :, channels : channels + 3, 0].astype(jnp.int32)
    kept = (arrived_tags[:, :, 1] == me) & (
        arrived_tags[:, :, 2] == jnp.arange(slot_count, dtype=jnp.int32)[None, :]
    )
    hit = (
        kept[:, :, None] & (arrived_tags[:, :, 0][:, :, None] == jnp.arange(rounds, dtype=jnp.int32)[None, None, :])
    ).astype(jnp.bfloat16)

    sub = 8
    blocks = (channels + meta_rows) // sub
    spread = jnp.where(same, hit.reshape(twin_count * slot_count, rounds).T[None, :, :, None], jnp.zeros((), jnp.bfloat16))
    stacked = arrived.reshape(twin_count * slot_count, blocks, sub, samples)
    noise = jnp.einsum("irjk,jbkq->birq", spread, stacked, preferred_element_type=jnp.float32)
    noise = noise.reshape(blocks * sub, rounds, samples)

    def cleaned_rows(lo, hi):
        return (record[lo:hi].astype(jnp.float32) - noise[lo:hi]).astype(jnp.bfloat16)

    def edge_row(c):
        edge_noise = jnp.einsum(
            "nsr,nsq->rq", hit, arrived[:, :, c], preferred_element_type=jnp.float32
        )
        return (record[c].astype(jnp.float32) - edge_noise).astype(jnp.bfloat16)[None]

    count = lax.axis_size("rcv")
    forward = [(i, i + 1) for i in range(count - 1)]
    backward = [(target, source) for source, target in forward]
    low = lax.ppermute(edge_row(channels - 1), "rcv", forward)
    high = lax.ppermute(edge_row(0), "rcv", backward)
    cleaned = cleaned_rows(0, channels)
    widened = jnp.concatenate([low, cleaned, high], axis=0).astype(jnp.float32)
    smooth = 0.5 * widened[1:-1] + 0.25 * (widened[:-2] + widened[2:])
    return smooth.astype(jnp.bfloat16)


def solution(mesh):
    placed = (P("rcv", None, "twin"), P("twin"), P("twin", None), P())
    return jax.shard_map(
        local, mesh=mesh, in_specs=placed, out_specs=P("rcv", None, "twin"), check_vma=False
    )
```

```python
import jax
import jax.numpy as jnp
from jax import lax
from jax.sharding import PartitionSpec as P


def pair_routes(slip_block, ghost_lag, twin_count):
    rec_count, order_count = ghost_lag.shape
    pair_total = rec_count * order_count
    target = (slip_block[:, None] - ghost_lag).reshape(pair_total)
    valid = target >= 0
    safe = jnp.maximum(target, 0)
    owner = jnp.where(valid, safe % twin_count, -1)
    land_round = safe // twin_count
    position = jnp.arange(pair_total, dtype=jnp.int32)
    earlier = (owner[None, :] == owner[:, None]) & (position[None, :] < position[:, None])
    slot = jnp.sum(earlier.astype(jnp.int32), axis=1)
    return owner, slot, land_round


def local(record, slip_block, ghost_lag, order_ops):
    twin_count = lax.axis_size("twin")
    channels, rounds, samples = record.shape
    rec_count, order_count = ghost_lag.shape
    pair_total = rec_count * order_count
    slot_count = pair_total // twin_count + 1

    count = lax.axis_size("rcv")
    forward = [(i, i + 1) for i in range(count - 1)]
    backward = [(target, source) for source, target in forward]
    prev_last = lax.ppermute(record[channels - 1], "rcv", forward)
    next_first = lax.ppermute(record[0], "rcv", backward)

    guides = jnp.take(record, slip_block // twin_count, axis=1, mode="clip")
    estimates = jnp.einsum(
        "crp,hpq->rhcq", guides, order_ops, preferred_element_type=jnp.float32
    ).astype(jnp.bfloat16)
    estimates = estimates.reshape(pair_total, channels, samples)

    owner, slot, land_round = pair_routes(slip_block, ghost_lag, twin_count)
    meta_rows = 8
    round_row = jnp.broadcast_to(land_round.astype(jnp.bfloat16)[:, None, None], (pair_total, 1, samples))
    edge_guides = jnp.take(jnp.stack([prev_last, next_first]), slip_block // twin_count, axis=1, mode="clip")
    edge_estimates = jnp.einsum(
        "erp,hpq->rheq", edge_guides, order_ops, preferred_element_type=jnp.float32
    ).astype(jnp.bfloat16).reshape(pair_total, 2, samples)
    meta = jnp.concatenate(
        [round_row, edge_estimates, jnp.zeros((pair_total, meta_rows - 3, samples), jnp.bfloat16)], axis=1
    )
    blank = jnp.zeros((1, channels + meta_rows, samples), jnp.bfloat16)
    tagged = jnp.concatenate([jnp.concatenate([estimates, meta], axis=1), blank], axis=0)
    chosen = (owner[:, None, None] == jnp.arange(twin_count, dtype=jnp.int32)[None, :, None]) & (
        slot[:, None, None] == jnp.arange(slot_count, dtype=jnp.int32)[None, None, :]
    )
    pick = jnp.where(jnp.any(chosen, axis=0), jnp.argmax(chosen, axis=0), pair_total)
    outgoing = jnp.take(tagged, pick.reshape(twin_count * slot_count), axis=0, mode="clip")
    outgoing = outgoing.reshape(twin_count, slot_count * (channels + meta_rows), samples)
    sub = 8
    same = lax.broadcasted_iota(jnp.int32, (sub, 1, 1, sub), 0) == lax.broadcasted_iota(jnp.int32, (sub, 1, 1, sub), 3)
    outgoing, same, prev_last, next_first = lax.optimization_barrier((outgoing, same, prev_last, next_first))
    arrived = lax.all_to_all(outgoing, "twin", split_axis=0, concat_axis=0, tiled=True)
    arrived = arrived.reshape(twin_count, slot_count, channels + meta_rows, samples)

    arrived_rounds = arrived[:, :, channels, 0].astype(jnp.int32)
    hit = (arrived_rounds[:, :, None] == jnp.arange(rounds, dtype=jnp.int32)[None, None, :]).astype(jnp.bfloat16)

    sub = 8
    blocks = (channels + meta_rows) // sub
    spread = jnp.where(same, hit.reshape(twin_count * slot_count, rounds).T[None, :, :, None], jnp.zeros((), jnp.bfloat16))
    stacked = arrived.reshape(twin_count * slot_count, blocks, sub, samples)
    noise = jnp.einsum("irjk,jbkq->birq", spread, stacked, preferred_element_type=jnp.float32)
    noise = noise.reshape(blocks * sub, rounds, samples)

    def cleaned_rows(lo, hi):
        return (record[lo:hi].astype(jnp.float32) - noise[lo:hi]).astype(jnp.bfloat16)

    def halo_row(row, neighbour):
        edge_noise = jnp.einsum(
            "nsr,nsq->rq", hit, arrived[:, :, row], preferred_element_type=jnp.float32
        )
        return (neighbour.astype(jnp.float32) - edge_noise).astype(jnp.bfloat16)[None]

    low = halo_row(channels + 1, prev_last)
    high = halo_row(channels + 2, next_first)
    cleaned = cleaned_rows(0, channels)
    widened = jnp.concatenate([low, cleaned, high], axis=0).astype(jnp.float32)
    smooth = 0.5 * widened[1:-1] + 0.25 * (widened[:-2] + widened[2:])
    return smooth.astype(jnp.bfloat16)


def solution(mesh):
    placed = (P("rcv", None, "twin"), P("twin"), P("twin", None), P())
    return jax.shard_map(
        local, mesh=mesh, in_specs=placed, out_specs=P("rcv", None, "twin"), check_vma=False
    )
```

```python
import jax
import jax.numpy as jnp
from jax import lax
from jax.sharding import PartitionSpec as P


def pair_routes(slip_block, ghost_lag, twin_count):
    rec_count, order_count = ghost_lag.shape
    pair_total = rec_count * order_count
    target = (slip_block[:, None] - ghost_lag).reshape(pair_total)
    valid = target >= 0
    safe = jnp.maximum(target, 0)
    owner = jnp.where(valid, safe % twin_count, -1)
    land_round = safe // twin_count
    position = jnp.arange(pair_total, dtype=jnp.int32)
    earlier = (owner[None, :] == owner[:, None]) & (position[None, :] < position[:, None])
    slot = jnp.sum(earlier.astype(jnp.int32), axis=1)
    return owner, slot, land_round


def local(record, slip_block, ghost_lag, order_ops):
    twin_count = lax.axis_size("twin")
    channels, rounds, samples = record.shape
    rec_count, order_count = ghost_lag.shape
    pair_total = rec_count * order_count
    slot_count = pair_total // twin_count + 1

    count = lax.axis_size("rcv")
    forward = [(i, i + 1) for i in range(count - 1)]
    backward = [(target, source) for source, target in forward]
    prev_last = lax.ppermute(record[channels - 1], "rcv", forward)
    next_first = lax.ppermute(record[0], "rcv", backward)

    guides = jnp.take(record, slip_block // twin_count, axis=1, mode="clip")
    estimates = jnp.einsum(
        "crp,hpq->rhcq", guides, order_ops, preferred_element_type=jnp.float32
    ).astype(jnp.bfloat16)
    estimates = estimates.reshape(pair_total, channels, samples)

    owner, slot, land_round = pair_routes(slip_block, ghost_lag, twin_count)
    meta_rows = 8
    tag_rows = jnp.broadcast_to(
        jnp.stack([land_round, owner, slot], axis=1).astype(jnp.bfloat16)[:, :, None], (pair_total, 3, samples)
    )
    edge_guides = jnp.take(jnp.stack([prev_last, next_first]), slip_block // twin_count, axis=1, mode="clip")
    edge_estimates = jnp.einsum(
        "erp,hpq->rheq", edge_guides, order_ops, preferred_element_type=jnp.float32
    ).astype(jnp.bfloat16).reshape(pair_total, 2, samples)
    meta = jnp.concatenate(
        [tag_rows, edge_estimates, jnp.zeros((pair_total, meta_rows - 5, samples), jnp.bfloat16)], axis=1
    )
    tagged = jnp.concatenate([estimates, meta], axis=1)
    chosen = (owner[:, None, None] == jnp.arange(twin_count, dtype=jnp.int32)[None, :, None]) & (
        slot[:, None, None] == jnp.arange(slot_count, dtype=jnp.int32)[None, None, :]
    )
    pick = jnp.argmax(chosen, axis=0)
    outgoing = jnp.take(tagged, pick.reshape(twin_count * slot_count), axis=0, mode="clip")
    outgoing = outgoing.reshape(twin_count, slot_count * (channels + meta_rows), samples)
    sub = 8
    same = lax.broadcasted_iota(jnp.int32, (sub, 1, 1, sub), 0) == lax.broadcasted_iota(jnp.int32, (sub, 1, 1, sub), 3)
    me = lax.axis_index("twin")
    outgoing, same, me, prev_last, next_first = lax.optimization_barrier((outgoing, same, me, prev_last, next_first))
    arrived = lax.all_to_all(outgoing, "twin", split_axis=0, concat_axis=0, tiled=True)
    arrived = arrived.reshape(twin_count, slot_count, channels + meta_rows, samples)

    arrived_tags = arrived[:, :, channels : channels + 3, 0].astype(jnp.int32)
    kept = (arrived_tags[:, :, 1] == me) & (
        arrived_tags[:, :, 2] == jnp.arange(slot_count, dtype=jnp.int32)[None, :]
    )
    hit = (
        kept[:, :, None] & (arrived_tags[:, :, 0][:, :, None] == jnp.arange(rounds, dtype=jnp.int32)[None, None, :])
    ).astype(jnp.bfloat16)

    sub = 8
    blocks = (channels + meta_rows) // sub
    spread = jnp.where(same, hit.reshape(twin_count * slot_count, rounds).T[None, :, :, None], jnp.zeros((), jnp.bfloat16))
    stacked = arrived.reshape(twin_count * slot_count, blocks, sub, samples)
    noise = jnp.einsum("irjk,jbkq->birq", spread, stacked, preferred_element_type=jnp.float32)
    noise = noise.reshape(blocks * sub, rounds, samples)

    def cleaned_rows(lo, hi):
        return (record[lo:hi].astype(jnp.float32) - noise[lo:hi]).astype(jnp.bfloat16)

    def halo_row(row, neighbour):
        edge_noise = jnp.einsum(
            "nsr,nsq->rq", hit, arrived[:, :, row], preferred_element_type=jnp.float32
        )
        return (neighbour.astype(jnp.float32) - edge_noise).astype(jnp.bfloat16)[None]

    low = halo_row(channels + 3, prev_last)
    high = halo_row(channels + 4, next_first)
    cleaned = cleaned_rows(0, channels)
    widened = jnp.concatenate([low, cleaned, high], axis=0).astype(jnp.float32)
    smooth = 0.5 * widened[1:-1] + 0.25 * (widened[:-2] + widened[2:])
    return smooth.astype(jnp.bfloat16)


def solution(mesh):
    placed = (P("rcv", None, "twin"), P("twin"), P("twin", None), P())
    return jax.shard_map(
        local, mesh=mesh, in_specs=placed, out_specs=P("rcv", None, "twin"), check_vma=False
    )
```

```python
import jax
import jax.numpy as jnp
from jax import lax
from jax.sharding import PartitionSpec as P


def pair_routes(slip_block, ghost_lag, twin_count):
    rec_count, order_count = ghost_lag.shape
    pair_total = rec_count * order_count
    target = (slip_block[:, None] - ghost_lag).reshape(pair_total)
    valid = target >= 0
    safe = jnp.maximum(target, 0)
    owner = jnp.where(valid, safe % twin_count, -1)
    land_round = safe // twin_count
    position = jnp.arange(pair_total, dtype=jnp.int32)
    earlier = (owner[None, :] == owner[:, None]) & (position[None, :] < position[:, None])
    slot = jnp.sum(earlier.astype(jnp.int32), axis=1)
    return owner, slot, land_round


def local(record, slip_block, ghost_lag, order_ops):
    twin_count = lax.axis_size("twin")
    channels, rounds, samples = record.shape
    table = lax.optimization_barrier(jnp.concatenate([slip_block[:, None], ghost_lag], axis=1))
    slip_block, ghost_lag = table[:, 0], table[:, 1:]
    rec_count, order_count = ghost_lag.shape
    pair_total = rec_count * order_count
    slot_count = pair_total // twin_count + 1

    guides = jnp.take(record, slip_block // twin_count, axis=1, mode="clip")
    estimates = jnp.einsum(
        "crp,hpq->rhcq", guides, order_ops, preferred_element_type=jnp.float32
    ).astype(jnp.bfloat16)
    estimates = estimates.reshape(pair_total, channels, samples)

    owner, slot, land_round = pair_routes(slip_block, ghost_lag, twin_count)
    meta_rows = 8
    meta = jnp.broadcast_to(land_round.astype(jnp.bfloat16)[:, None, None], (pair_total, meta_rows, samples))
    blank = jnp.zeros((1, channels + meta_rows, samples), jnp.bfloat16)
    tagged = jnp.concatenate([jnp.concatenate([estimates, meta], axis=1), blank], axis=0)
    chosen = (owner[:, None, None] == jnp.arange(twin_count, dtype=jnp.int32)[None, :, None]) & (
        slot[:, None, None] == jnp.arange(slot_count, dtype=jnp.int32)[None, None, :]
    )
    pick = jnp.where(jnp.any(chosen, axis=0), jnp.argmax(chosen, axis=0), pair_total)
    outgoing = jnp.take(tagged, pick.reshape(twin_count * slot_count), axis=0, mode="clip")
    outgoing = outgoing.reshape(twin_count, slot_count * (channels + meta_rows), samples)
    sub = 8
    same = lax.broadcasted_iota(jnp.int32, (sub, 1, 1, sub), 0) == lax.broadcasted_iota(jnp.int32, (sub, 1, 1, sub), 3)
    outgoing, same = lax.optimization_barrier((outgoing, same))
    arrived = lax.all_to_all(outgoing, "twin", split_axis=0, concat_axis=0, tiled=True)
    arrived = arrived.reshape(twin_count, slot_count, channels + meta_rows, samples)

    arrived_rounds = arrived[:, :, channels, 0].astype(jnp.int32)
    hit = (arrived_rounds[:, :, None] == jnp.arange(rounds, dtype=jnp.int32)[None, None, :]).astype(jnp.bfloat16)

    sub = 8
    blocks = (channels + meta_rows) // sub
    spread = jnp.where(same, hit.reshape(twin_count * slot_count, rounds).T[None, :, :, None], jnp.zeros((), jnp.bfloat16))
    stacked = arrived.reshape(twin_count * slot_count, blocks, sub, samples)
    noise = jnp.einsum("irjk,jbkq->birq", spread, stacked, preferred_element_type=jnp.float32)
    noise = noise.reshape(blocks * sub, rounds, samples)

    def cleaned_rows(lo, hi):
        return (record[lo:hi].astype(jnp.float32) - noise[lo:hi]).astype(jnp.bfloat16)

    def edge_row(c):
        edge_noise = jnp.einsum(
            "nsr,nsq->rq", hit, arrived[:, :, c], preferred_element_type=jnp.float32
        )
        return (record[c].astype(jnp.float32) - edge_noise).astype(jnp.bfloat16)[None]

    count = lax.axis_size("rcv")
    forward = [(i, i + 1) for i in range(count - 1)]
    backward = [(target, source) for source, target in forward]
    low = lax.ppermute(edge_row(channels - 1), "rcv", forward)
    high = lax.ppermute(edge_row(0), "rcv", backward)
    cleaned = cleaned_rows(0, channels)
    widened = jnp.concatenate([low, cleaned, high], axis=0).astype(jnp.float32)
    smooth = 0.5 * widened[1:-1] + 0.25 * (widened[:-2] + widened[2:])
    return smooth.astype(jnp.bfloat16)


def solution(mesh):
    placed = (P("rcv", None, "twin"), P("twin"), P("twin", None), P())
    return jax.shard_map(
        local, mesh=mesh, in_specs=placed, out_specs=P("rcv", None, "twin"), check_vma=False
    )
```
